512 devices in a mesh: seg: 32 (over y, x), sec: 16 (over z, core).
Axes of the slice: x: 4, y: 8, z: 8, core: 2. Of those that a mesh axis runs over, the one named last changes fastest.
Arguments:
- blocks: bfloat16 [32, 4, 16, 128, 128], P('seg', None, 'sec'), may hold values from -0.5 to 0.5
- left_edge: bfloat16 [16, 128], P('sec'), may hold values from -0.5 to 0.5
- right_edge: bfloat16 [16, 128], P('sec'), may hold values from -6 to 6
- occupation: int32 [1024, 32], P(None, 'seg'), may hold values from 0 to 3
- start_sector: int32 [1024], replicated, may hold values from 0 to 15
Outputs:
- amplitude: float32 [1024], replicated
The draws below stay inside these ranges and needn't reach their ends.
All inputs are finite; a program needn't handle non-finite values.
Results may differ from the reference program's by a relative error of at most 0.015.
Values may be sent and summed in bfloat16 or wider, within the bound.
No kernel may reach another device: no remote copies, remote signals or barrier semaphores. Data moves between devices by JAX's collectives and lax.ppermute only.
A program may use at most 64 MiB of HBM per device.

```python
import jax
import jax.numpy as jnp

SW = 128
NSEC = 16
LOCAL = 4
SITES = 32
MID = 16
CONF = 1024


def plant(drawn, rng, low, high):
    shape = drawn.shape
    place = [jax.random.randint(jax.random.fold_in(rng, axis), (), 0, shape[axis]) for axis in range(len(shape))]
    drawn = drawn.at[tuple(place)].set(low)
    longest = shape.index(max(shape))
    place[longest] = (place[longest] + 1) % shape[longest]
    return drawn.at[tuple(place)].set(high)


def shard_levels(own_key, extent, pieces, least, top_value):
    factor_of = 1.0
    for position, shards_of in pieces:
        draws = jax.random.uniform(jax.random.fold_in(jax.random.fold_in(own_key, 6), position), (shards_of,), jnp.float32, least / len(pieces), top_value / len(pieces))
        factor_of = factor_of * jnp.repeat(jnp.exp(draws), extent[position] // shards_of).reshape((-1,) + (1,) * (len(extent) - 1 - position))
    return factor_of


def gaussian(rng, extent, deviation, most, split=(), held_as=jnp.bfloat16):
    values = deviation * jax.random.normal(rng, extent, jnp.float32)
    if split:
        values = values * shard_levels(rng, extent, split, -0.22, 0.18)
    return jnp.clip(values, -most, most).astype(held_as)


def setup_inputs(seed: int = 0) -> dict:
    seeds = jax.random.split(jax.random.key(seed), 6)
    blocks = gaussian(seeds[0], (SITES, LOCAL, NSEC, SW, SW), SW ** -0.5, 0.5, ((0, 32), (2, 16)))
    left_edge = gaussian(seeds[1], (NSEC, SW), SW ** -0.5, 0.5, ((0, 16),))
    right_edge = gaussian(seeds[2], (NSEC, SW), 1.0, 6.0, ((0, 16),))
    occupation = plant(jax.random.randint(seeds[3], (CONF, SITES), 0, 4), jax.random.fold_in(seeds[3], 1), 0, 3).astype(jnp.int32)
    start_sector = plant(jax.random.randint(seeds[4], (CONF,), 0, NSEC), jax.random.fold_in(seeds[4], 1), 0, NSEC - 1).astype(jnp.int32)
    return dict(blocks=blocks, left_edge=left_edge, right_edge=right_edge, occupation=occupation, start_sector=start_sector)


def reference(blocks, left_edge, right_edge, occupation, start_sector):
    charge = jnp.array([0, 1, -1, 0], dtype=jnp.int32)
    charge_step = charge[occupation]
    running = jnp.cumsum(charge_step, axis=1).astype(jnp.int32)
    first_col = jnp.zeros((occupation.shape[0], 1), dtype=jnp.int32)
    sector = (start_sector[:, None] + jnp.concatenate([first_col, running], axis=1)) % NSEC
    sector = sector.astype(jnp.int32)
    left_env = left_edge[sector[:, 0]]
    for site_index in range(MID):
        chosen = blocks[site_index][occupation[:, site_index], sector[:, site_index]]
        left_env = jnp.einsum("ka,kab->kb", left_env.astype(jnp.float32), chosen.astype(jnp.float32)).astype(jnp.bfloat16)
    right_env = right_edge[sector[:, SITES]]
    for site_index in range(SITES - 1, MID - 1, -1):
        chosen = blocks[site_index][occupation[:, site_index], sector[:, site_index]]
        right_env = jnp.einsum("kab,kb->ka", chosen.astype(jnp.float32), right_env.astype(jnp.float32)).astype(jnp.bfloat16)
    return jnp.sum(left_env.astype(jnp.float32) * right_env.astype(jnp.float32), axis=1)
```

```python
import jax
import jax.numpy as jnp
from jax import lax
from jax.sharding import PartitionSpec as P


def per_device(blocks, left_edge, right_edge, occupation, start_sector):
    seg_count = lax.axis_size("seg")
    sec_count = lax.axis_size("sec")
    half_count = seg_count // 2
    seg_index = lax.axis_index("seg")
    sec_index = lax.axis_index("sec")
    is_left = seg_index < half_count
    depth = jnp.where(is_left, seg_index, seg_count - 1 - seg_index)

    conf_count = occupation.shape[0]
    sites = seg_count * occupation.shape[1]
    group = conf_count // sec_count
    width = blocks.shape[-1]
    local_states = blocks.shape[1]

    site_blocks = lax.all_gather(blocks[0], "sec", axis=1, tiled=True)
    nsec = site_blocks.shape[1]
    lefts = lax.all_gather(left_edge, "sec", axis=0, tiled=True)
    rights = lax.all_gather(right_edge, "sec", axis=0, tiled=True)

    row0 = sec_index * group
    occ_mine = lax.dynamic_slice_in_dim(occupation, row0, group, axis=0)
    occ_group = lax.all_gather(occ_mine, "seg", axis=1, tiled=True)
    start_group = lax.dynamic_slice_in_dim(start_sector, row0, group, axis=0)

    charge = jnp.array([0, 1, -1, 0], dtype=jnp.int32)
    steps = charge[occ_group]
    site_ids = jnp.arange(sites, dtype=jnp.int32)
    before = jnp.sum(jnp.where(site_ids[None, :] < seg_index, steps, 0), axis=1)
    total = jnp.sum(steps, axis=1)
    sector_here = jnp.mod(start_group + before, nsec)
    sector_end = jnp.mod(start_group + total, nsec)
    occ_here = occ_mine[:, 0]

    sector_hot = (sector_here[:, None] == jnp.arange(nsec, dtype=jnp.int32)[None, :]).astype(
        jnp.bfloat16
    )
    state_hot = (occ_here[:, None] == jnp.arange(local_states, dtype=jnp.int32)[None, :]).astype(
        jnp.float32
    )

    oriented = lax.cond(
        is_left,
        lambda b: b,
        lambda b: jnp.swapaxes(b, 2, 3),
        site_blocks,
    )

    def apply(vector):
        spread = vector[:, None, :] * sector_hot[:, :, None]
        products = jnp.einsum(
            "kqa,nqab->knb", spread, oriented, preferred_element_type=jnp.float32
        )
        return jnp.sum(products * state_hot[:, :, None], axis=1).astype(jnp.bfloat16)

    first_left = jnp.take(lefts, start_group, axis=0)
    first_right = jnp.take(rights, sector_end, axis=0)
    first = jnp.where(is_left, first_left, first_right)
    vector = jnp.where(depth == 0, first, jnp.zeros_like(first))

    chain = [(j, j + 1) for j in range(half_count - 1)] + [
        (j, j - 1) for j in range(half_count + 1, seg_count)
    ]
    for step in range(half_count):
        vector = apply(vector)
        if step < half_count - 1:
            vector = lax.ppermute(vector, "seg", chain)

    meet = [(half_count - 1, half_count), (half_count, half_count - 1)]
    other = lax.ppermute(vector, "seg", meet)
    amp = jnp.sum(vector.astype(jnp.float32) * other.astype(jnp.float32), axis=1)
    amp = jnp.where(seg_index == half_count - 1, amp, jnp.zeros_like(amp))
    gathered = lax.all_gather(amp, "sec", axis=0, tiled=True)
    return lax.psum(gathered, "seg")


def solution(mesh):
    in_specs = (
        P("seg", None, "sec", None, None),
        P("sec", None),
        P("sec", None),
        P(None, "seg"),
        P(),
    )
    out_specs = P()
    return jax.shard_map(
        per_device, mesh=mesh, in_specs=in_specs, out_specs=out_specs, check_vma=False
    )
```

```python
import jax
import jax.numpy as jnp
from jax import lax
from jax.sharding import PartitionSpec as P


def exchange_rounds(value, axis, partner_sets):
    total = value
    for pairs in partner_sets:
        if pairs:
            total = total + lax.ppermute(value, axis, pairs)
    return total


def per_device(blocks, left_edge, right_edge, occupation, start_sector):
    seg_count = lax.axis_size("seg")
    sec_count = lax.axis_size("sec")
    half_count = seg_count // 2
    seg_index = lax.axis_index("seg")
    sec_index = lax.axis_index("sec")
    is_left = seg_index < half_count
    depth = jnp.where(is_left, seg_index, seg_count - 1 - seg_index)

    conf_count = occupation.shape[0]
    sites = seg_count * occupation.shape[1]
    group = conf_count // sec_count
    width = blocks.shape[-1]
    local_states = blocks.shape[1]

    rows = blocks[0, :, 0].reshape(local_states * width, width)
    pad = jnp.zeros((14, width), blocks.dtype)
    packed = jnp.concatenate([rows, left_edge, right_edge, pad], axis=0)
    gathered = lax.all_gather(packed, "sec", axis=0, tiled=False)
    nsec = gathered.shape[0]
    body = local_states * width
    site_blocks = gathered[:, :body].reshape(nsec, local_states, width, width)
    lefts = gathered[:, body]
    rights = gathered[:, body + 1]

    row0 = sec_index * group
    occ_mine = lax.dynamic_slice_in_dim(occupation, row0, group, axis=0)
    occ_group = lax.all_gather(occ_mine, "seg", axis=1, tiled=True)
    start_group = lax.dynamic_slice_in_dim(start_sector, row0, group, axis=0)

    charge = jnp.array([0, 1, -1, 0], dtype=jnp.int32)
    steps = charge[occ_group]
    site_ids = jnp.arange(sites, dtype=jnp.int32)
    before = jnp.sum(jnp.where(site_ids[None, :] < seg_index, steps, 0), axis=1)
    total = jnp.sum(steps, axis=1)
    sector_here = jnp.mod(start_group + before, nsec)
    sector_end = jnp.mod(start_group + total, nsec)
    occ_here = occ_mine[:, 0]

    sector_hot = (sector_here[:, None] == jnp.arange(nsec, dtype=jnp.int32)[None, :]).astype(
        jnp.bfloat16
    )
    state_hot = (occ_here[:, None] == jnp.arange(local_states, dtype=jnp.int32)[None, :]).astype(
        jnp.float32
    )

    oriented = lax.cond(
        is_left,
        lambda b: b,
        lambda b: jnp.swapaxes(b, 2, 3),
        site_blocks,
    )

    def apply(vector):
        spread = vector[:, None, :] * sector_hot[:, :, None]
        products = jnp.einsum(
            "kqa,qnab->knb", spread, oriented, preferred_element_type=jnp.float32
        )
        return jnp.sum(products * state_hot[:, :, None], axis=1).astype(jnp.bfloat16)

    first_left = jnp.take(lefts, start_group, axis=0)
    first_right = jnp.take(rights, sector_end, axis=0)
    first = jnp.where(is_left, first_left, first_right)
    vector = jnp.where(depth == 0, first, jnp.zeros_like(first))

    chain = [(j, j + 1) for j in range(half_count - 1)] + [
        (j, j - 1) for j in range(half_count + 1, seg_count)
    ]
    for step in range(half_count):
        vector = apply(vector)
        if step < half_count - 1:
            vector = lax.ppermute(vector, "seg", chain)

    low, high = half_count - 1, half_count
    other = lax.ppermute(vector, "seg", [(low, high), (high, low)])
    amp = jnp.sum(vector.astype(jnp.float32) * other.astype(jnp.float32), axis=1)
    at_meet = (seg_index == low) | (seg_index == high)
    amp = jnp.where(at_meet, amp, jnp.zeros_like(amp))

    pieces = amp[None, :]
    span = 1
    while span < sec_count:
        own_slot = (sec_index // span) % 4
        parts = [pieces]
        for t in (1, 2, 3):
            pairs = [(i, i ^ (t * span)) for i in range(sec_count)]
            parts.append(lax.ppermute(pieces, "sec", pairs))
        slots = []
        for r in range(4):
            chosen = jnp.zeros_like(pieces)
            for t in range(4):
                chosen = chosen + jnp.where(own_slot ^ t == r, parts[t], jnp.zeros_like(pieces))
            slots.append(chosen)
        pieces = jnp.concatenate(slots, axis=0)
        span *= 4
    full = pieces.reshape(conf_count)

    def outward(offset, holders):
        pairs = []
        for h in holders:
            target = h - offset if h <= low else h + offset
            if 0 <= target < seg_count:
                pairs.append((h, target))
        return pairs

    holders = [low, high]
    for offsets in ((1, 2, 3), (4, 8, 12)):
        full = exchange_rounds(full, "seg", [outward(o, holders) for o in offsets])
        holders = sorted(set(holders) | {t for o in offsets for _, t in outward(o, holders)})
    return full


def solution(mesh):
    in_specs = (
        P("seg", None, "sec", None, None),
        P("sec", None),
        P("sec", None),
        P(None, "seg"),
        P(),
    )
    out_specs = P()
    return jax.shard_map(
        per_device, mesh=mesh, in_specs=in_specs, out_specs=out_specs, check_vma=False
    )
```

```python
import jax
import jax.numpy as jnp
from jax import lax
from jax.sharding import PartitionSpec as P


def spread_pairs(holders, count, fan):
    have = sorted(holders)
    rounds = []
    while len(have) < count:
        missing = [i for i in range(count) if i not in have]
        perms = []
        for _ in range(fan):
            pairs = []
            for h in have:
                if not missing:
                    break
                target = min(missing, key=lambda m: (abs(m - h), m))
                missing.remove(target)
                pairs.append((h, target))
            if pairs:
                perms.append(pairs)
        rounds.append(perms)
        have = sorted(set(have) | {t for perm in perms for _, t in perm})
    return rounds


def per_device(blocks, left_edge, right_edge, occupation, start_sector):
    seg_count = lax.axis_size("seg")
    sec_count = lax.axis_size("sec")
    half_count = seg_count // 2
    seg_index = lax.axis_index("seg")
    sec_index = lax.axis_index("sec")
    is_left = seg_index < half_count
    partner = seg_index ^ 1
    depth = jnp.where(is_left, seg_index // 2, (seg_count - 1 - seg_index) // 2)

    conf_count = occupation.shape[0]
    sites = seg_count * occupation.shape[1]
    group = conf_count // sec_count
    width = blocks.shape[-1]
    local_states = blocks.shape[1]

    rows = blocks[0, :, 0].reshape(local_states * width, width)
    pad = jnp.zeros((14, width), blocks.dtype)
    packed = jnp.concatenate([rows, left_edge, right_edge, pad], axis=0)
    gathered = lax.all_gather(packed, "sec", axis=0, tiled=False)
    nsec = gathered.shape[0]
    body = local_states * width
    lefts = gathered[:, body]
    rights = gathered[:, body + 1]

    feed = [(2 * m + 1, 2 * m) for m in range(half_count // 2)] + [
        (2 * m, 2 * m + 1) for m in range(half_count // 2, seg_count // 2)
    ]
    partner_gathered = lax.ppermute(gathered[:, :body], "seg", feed)

    def arrange(transpose):
        def build(own, other):
            pair = []
            for part in (own[:, :body], other):
                part = part.reshape(nsec, local_states, width, width)
                pair.append(jnp.swapaxes(part, 2, 3) if transpose else part)
            return tuple(pair)

        return build

    oriented = lax.cond(is_left, arrange(False), arrange(True), gathered, partner_gathered)

    row0 = sec_index * group
    occ_mine = lax.dynamic_slice_in_dim(occupation, row0, group, axis=0)
    occ_group = lax.all_gather(occ_mine, "seg", axis=1, tiled=True)
    start_group = lax.dynamic_slice_in_dim(start_sector, row0, group, axis=0)

    charge = jnp.array([0, 1, -1, 0], dtype=jnp.int32)
    steps = charge[occ_group]
    site_ids = jnp.arange(sites, dtype=jnp.int32)
    total = jnp.sum(steps, axis=1)
    sector_end = jnp.mod(start_group + total, nsec)
    sector_ids = jnp.arange(nsec, dtype=jnp.int32)
    state_ids = jnp.arange(local_states, dtype=jnp.int32)

    def site_masks(site):
        before = jnp.sum(jnp.where(site_ids[None, :] < site, steps, 0), axis=1)
        sector = jnp.mod(start_group + before, nsec)
        occ = jnp.sum(jnp.where(site_ids[None, :] == site, occ_group, 0), axis=1)
        sector_hot = (sector[:, None] == sector_ids[None, :]).astype(jnp.bfloat16)
        state_hot = (occ[:, None] == state_ids[None, :]).astype(jnp.float32)
        return sector_hot, state_hot

    masks = [site_masks(seg_index), site_masks(partner)]

    def apply(vector, which):
        sector_hot, state_hot = masks[which]
        spread = vector[:, None, :] * sector_hot[:, :, None]
        products = jnp.einsum(
            "kqa,qnab->knb", spread, oriented[which], preferred_element_type=jnp.float32
        )
        return jnp.sum(products * state_hot[:, :, None], axis=1).astype(jnp.bfloat16)

    first_left = jnp.take(lefts, start_group, axis=0)
    first_right = jnp.take(rights, sector_end, axis=0)
    first = jnp.where(is_left, first_left, first_right)
    vector = jnp.where(depth == 0, first, jnp.zeros_like(first))

    chain = [(j, j + 2) for j in range(0, half_count - 2, 2)] + [
        (j, j - 2) for j in range(half_count + 3, seg_count, 2)
    ]
    chain_steps = half_count // 2
    for step in range(chain_steps):
        vector = apply(vector, 0)
        vector = apply(vector, 1)
        if step < chain_steps - 1:
            vector = lax.ppermute(vector, "seg", chain)

    low, high = half_count - 2, half_count + 1
    other = lax.ppermute(vector, "seg", [(low, high), (high, low)])
    amp = jnp.sum(vector.astype(jnp.float32) * other.astype(jnp.float32), axis=1)
    at_meet = (seg_index == low) | (seg_index == high)
    amp = jnp.where(at_meet, amp, jnp.zeros_like(amp))

    pieces = amp[None, :]
    span = 1
    while span < sec_count:
        own_slot = (sec_index // span) % 4
        parts = [pieces]
        for t in (1, 2, 3):
            pairs = [(i, i ^ (t * span)) for i in range(sec_count)]
            parts.append(lax.ppermute(pieces, "sec", pairs))
        slots = []
        for r in range(4):
            chosen = jnp.zeros_like(pieces)
            for t in range(4):
                chosen = chosen + jnp.where(own_slot ^ t == r, parts[t], jnp.zeros_like(pieces))
            slots.append(chosen)
        pieces = jnp.concatenate(slots, axis=0)
        span *= 4
    full = pieces.reshape(conf_count)

    for perms in spread_pairs([low, high], seg_count, 3):
        received = [lax.ppermute(full, "seg", pairs) for pairs in perms]
        for value in received:
            full = full + value
    return full


def solution(mesh):
    in_specs = (
        P("seg", None, "sec", None, None),
        P("sec", None),
        P("sec", None),
        P(None, "seg"),
        P(),
    )
    out_specs = P()
    return jax.shard_map(
        per_device, mesh=mesh, in_specs=in_specs, out_specs=out_specs, check_vma=False
    )
```

```python
import jax
import jax.numpy as jnp
from jax import lax
from jax.sharding import PartitionSpec as P


def exchange_rounds(value, axis, partner_sets):
    total = value
    for pairs in partner_sets:
        if pairs:
            total = total + lax.ppermute(value, axis, pairs)
    return total


def per_device(blocks, left_edge, right_edge, occupation, start_sector):
    seg_count = lax.axis_size("seg")
    sec_count = lax.axis_size("sec")
    half_count = seg_count // 2
    seg_index = lax.axis_index("seg")
    sec_index = lax.axis_index("sec")
    is_left = seg_index < half_count
    depth = jnp.where(is_left, seg_index, seg_count - 1 - seg_index)

    conf_count = occupation.shape[0]
    sites = seg_count * occupation.shape[1]
    group = conf_count // sec_count
    width = blocks.shape[-1]
    local_states = blocks.shape[1]

    rows = blocks[0, :, 0].reshape(local_states * width, width)
    pad = jnp.zeros((14, width), blocks.dtype)
    packed = jnp.concatenate([rows, left_edge, right_edge, pad], axis=0)
    gathered = lax.all_gather(packed, "sec", axis=0, tiled=False)
    nsec = gathered.shape[0]
    body = local_states * width
    lefts = gathered[:, body]
    rights = gathered[:, body + 1]

    row0 = sec_index * group
    occ_mine = lax.dynamic_slice_in_dim(occupation, row0, group, axis=0)
    occ_group = lax.all_gather(occ_mine, "seg", axis=1, tiled=True)
    start_group = lax.dynamic_slice_in_dim(start_sector, row0, group, axis=0)

    charge = jnp.array([0, 1, -1, 0], dtype=jnp.int32)
    steps = charge[occ_group]
    site_ids = jnp.arange(sites, dtype=jnp.int32)
    before = jnp.sum(jnp.where(site_ids[None, :] < seg_index, steps, 0), axis=1)
    total = jnp.sum(steps, axis=1)
    sector_here = jnp.mod(start_group + before, nsec)
    sector_end = jnp.mod(start_group + total, nsec)
    occ_here = occ_mine[:, 0]

    sector_hot = (sector_here[:, None] == jnp.arange(nsec, dtype=jnp.int32)[None, :]).astype(
        jnp.bfloat16
    )
    state_hot = (occ_here[:, None] == jnp.arange(local_states, dtype=jnp.int32)[None, :]).astype(
        jnp.float32
    )

    def arrange(transpose):
        def build(rows_all):
            site_blocks = rows_all[:, :body].reshape(nsec, local_states, width, width)
            return jnp.swapaxes(site_blocks, 2, 3) if transpose else site_blocks

        return build

    oriented = lax.cond(is_left, arrange(False), arrange(True), gathered)

    def apply(vector):
        spread = vector[:, None, :] * sector_hot[:, :, None]
        products = jnp.einsum(
            "kqa,qnab->knb", spread, oriented, preferred_element_type=jnp.float32
        )
        return jnp.sum(products * state_hot[:, :, None], axis=1).astype(jnp.bfloat16)

    first_left = jnp.take(lefts, start_group, axis=0)
    first_right = jnp.take(rights, sector_end, axis=0)
    first = jnp.where(is_left, first_left, first_right)
    vector = jnp.where(depth == 0, first, jnp.zeros_like(first))

    chain = [(j, j + 1) for j in range(half_count - 1)] + [
        (j, j - 1) for j in range(half_count + 1, seg_count)
    ]
    for step in range(half_count):
        vector = apply(vector)
        if step < half_count - 1:
            vector = lax.ppermute(vector, "seg", chain)

    low, high = half_count - 1, half_count
    other = lax.ppermute(vector, "seg", [(low, high), (high, low)])
    amp = jnp.sum(vector.astype(jnp.float32) * other.astype(jnp.float32), axis=1)
    at_meet = (seg_index == low) | (seg_index == high)
    amp = jnp.where(at_meet, amp, jnp.zeros_like(amp))

    tile = jnp.zeros((8, width), jnp.float32).at[0, :group].set(amp)
    tiles = lax.all_gather(tile, "sec", axis=0, tiled=False)
    full = tiles[:, 0, :group].reshape(conf_count)

    def outward(offset, holders):
        pairs = []
        for h in holders:
            target = h - offset if h <= low else h + offset
            if 0 <= target < seg_count:
                pairs.append((h, target))
        return pairs

    holders = [low, high]
    for offsets in ((1, 2, 3), (4, 8, 12)):
        full = exchange_rounds(full, "seg", [outward(o, holders) for o in offsets])
        holders = sorted(set(holders) | {t for o in offsets for _, t in outward(o, holders)})
    return full


def solution(mesh):
    in_specs = (
        P("seg", None, "sec", None, None),
        P("sec", None),
        P("sec", None),
        P(None, "seg"),
        P(),
    )
    out_specs = P()
    return jax.shard_map(
        per_device, mesh=mesh, in_specs=in_specs, out_specs=out_specs, check_vma=False
    )
```

```python
import jax
import jax.numpy as jnp
from jax import lax
from jax.sharding import PartitionSpec as P


def exchange_rounds(value, axis, partner_sets):
    total = value
    for pairs in partner_sets:
        if pairs:
            total = total + lax.ppermute(value, axis, pairs)
    return total


def per_device(blocks, left_edge, right_edge, occupation, start_sector):
    seg_count = lax.axis_size("seg")
    sec_count = lax.axis_size("sec")
    half_count = seg_count // 2
    seg_index = lax.axis_index("seg")
    sec_index = lax.axis_index("sec")
    is_left = seg_index < half_count
    depth = jnp.where(is_left, seg_index, seg_count - 1 - seg_index)

    conf_count = occupation.shape[0]
    sites = seg_count * occupation.shape[1]
    group = conf_count // sec_count
    width = blocks.shape[-1]
    local_states = blocks.shape[1]

    rows = blocks[0, :, 0].reshape(local_states * width, width)
    pad = jnp.zeros((14, width), blocks.dtype)
    packed = jnp.concatenate([rows, left_edge, right_edge, pad], axis=0)
    gathered = lax.all_gather(packed, "sec", axis=0, tiled=False)
    nsec = gathered.shape[0]
    body = local_states * width
    lefts = gathered[:, body]
    rights = gathered[:, body + 1]

    row0 = sec_index * group
    occ_mine = lax.dynamic_slice_in_dim(occupation, row0, group, axis=0)
    occ_group = lax.all_gather(occ_mine, "seg", axis=1, tiled=True)
    start_group = lax.dynamic_slice_in_dim(start_sector, row0, group, axis=0)

    charge = jnp.array([0, 1, -1, 0], dtype=jnp.int32)
    steps = charge[occ_group]
    site_ids = jnp.arange(sites, dtype=jnp.int32)
    before = jnp.sum(jnp.where(site_ids[None, :] < seg_index, steps, 0), axis=1)
    total = jnp.sum(steps, axis=1)
    sector_here = jnp.mod(start_group + before, nsec)
    sector_end = jnp.mod(start_group + total, nsec)
    occ_here = occ_mine[:, 0]

    sector_hot = (sector_here[:, None] == jnp.arange(nsec, dtype=jnp.int32)[None, :]).astype(
        jnp.bfloat16
    )
    state_hot = (occ_here[:, None] == jnp.arange(local_states, dtype=jnp.int32)[None, :]).astype(
        jnp.float32
    )

    def arrange(transpose):
        def build(rows_all):
            site_blocks = rows_all[:, :body].reshape(nsec, local_states, width, width)
            return jnp.swapaxes(site_blocks, 2, 3) if transpose else site_blocks

        return build

    oriented = lax.cond(is_left, arrange(False), arrange(True), gathered)

    def apply(vector):
        spread = vector[:, None, :] * sector_hot[:, :, None]
        products = jnp.einsum(
            "kqa,qnab->knb", spread, oriented, preferred_element_type=jnp.float32
        )
        return jnp.sum(products * state_hot[:, :, None], axis=1).astype(jnp.bfloat16)

    first_left = jnp.take(lefts, start_group, axis=0)
    first_right = jnp.take(rights, sector_end, axis=0)
    first = jnp.where(is_left, first_left, first_right)
    vector = jnp.where(depth == 0, first, jnp.zeros_like(first))

    for step in range(half_count):
        vector = apply(vector)
        if step < half_count - 1:
            hop = [(step, step + 1), (seg_count - 1 - step, seg_count - 2 - step)]
            vector = lax.ppermute(vector, "seg", hop)

    low, high = half_count - 1, half_count
    other = lax.ppermute(vector, "seg", [(low, high), (high, low)])
    amp = jnp.sum(vector.astype(jnp.float32) * other.astype(jnp.float32), axis=1)
    at_meet = (seg_index == low) | (seg_index == high)
    amp = jnp.where(at_meet, amp, jnp.zeros_like(amp))

    tile = jnp.zeros((8, width), jnp.float32).at[0, :group].set(amp)
    tiles = lax.all_gather(tile, "sec", axis=0, tiled=False)
    full = tiles[:, 0, :group].reshape(conf_count)

    def outward(offset, holders):
        pairs = []
        for h in holders:
            target = h - offset if h <= low else h + offset
            if 0 <= target < seg_count:
                pairs.append((h, target))
        return pairs

    holders = [low, high]
    for offsets in ((1, 2, 3), (4, 8, 12)):
        full = exchange_rounds(full, "seg", [outward(o, holders) for o in offsets])
        holders = sorted(set(holders) | {t for o in offsets for _, t in outward(o, holders)})
    return full


def solution(mesh):
    in_specs = (
        P("seg", None, "sec", None, None),
        P("sec", None),
        P("sec", None),
        P(None, "seg"),
        P(),
    )
    out_specs = P()
    return jax.shard_map(
        per_device, mesh=mesh, in_specs=in_specs, out_specs=out_specs, check_vma=False
    )
```

```python
import jax
import jax.numpy as jnp
from jax import lax
from jax.sharding import PartitionSpec as P


def exchange_rounds(value, axis, partner_sets):
    total = value
    for pairs in partner_sets:
        if pairs:
            total = total + lax.ppermute(value, axis, pairs)
    return total


def per_device(blocks, left_edge, right_edge, occupation, start_sector):
    seg_count = lax.axis_size("seg")
    sec_count = lax.axis_size("sec")
    half_count = seg_count // 2
    seg_index = lax.axis_index("seg")
    sec_index = lax.axis_index("sec")
    is_left = seg_index < half_count
    depth = jnp.where(is_left, seg_index, seg_count - 1 - seg_index)

    conf_count = occupation.shape[0]
    sites = seg_count * occupation.shape[1]
    group = conf_count // sec_count
    width = blocks.shape[-1]
    local_states = blocks.shape[1]

    local = blocks[0, :, 0]
    local = jnp.where(is_left, local, jnp.swapaxes(local, 1, 2))
    edges = jnp.concatenate(
        [left_edge, right_edge, jnp.zeros((width - 2, width), blocks.dtype)], axis=0
    )
    packed = jnp.concatenate([local, edges[None]], axis=0)
    oriented = lax.all_gather(packed, "sec", axis=0, tiled=False)
    nsec = oriented.shape[0]
    lefts = oriented[:, local_states, 0]
    rights = oriented[:, local_states, 1]

    row0 = sec_index * group
    occ_mine = lax.dynamic_slice_in_dim(occupation, row0, group, axis=0)
    occ_group = lax.all_gather(occ_mine, "seg", axis=1, tiled=True)
    start_group = lax.dynamic_slice_in_dim(start_sector, row0, group, axis=0)

    charge = jnp.array([0, 1, -1, 0], dtype=jnp.int32)
    steps = charge[occ_group]
    site_ids = jnp.arange(sites, dtype=jnp.int32)
    before = jnp.sum(jnp.where(site_ids[None, :] < seg_index, steps, 0), axis=1)
    total = jnp.sum(steps, axis=1)
    sector_here = jnp.mod(start_group + before, nsec)
    sector_end = jnp.mod(start_group + total, nsec)
    occ_here = occ_mine[:, 0]

    sector_hot = (sector_here[:, None] == jnp.arange(nsec, dtype=jnp.int32)[None, :]).astype(
        jnp.bfloat16
    )
    state_hot = (occ_here[:, None] == jnp.arange(local_states + 1, dtype=jnp.int32)[None, :]).astype(
        jnp.float32
    )

    def apply(vector):
        spread = vector[:, None, :] * sector_hot[:, :, None]
        products = jnp.einsum(
            "kqa,qnab->knb", spread, oriented, preferred_element_type=jnp.float32
        )
        return jnp.sum(products * state_hot[:, :, None], axis=1).astype(jnp.bfloat16)

    first_left = jnp.take(lefts, start_group, axis=0)
    first_right = jnp.take(rights, sector_end, axis=0)
    first = jnp.where(is_left, first_left, first_right)
    vector = jnp.where(depth == 0, first, jnp.zeros_like(first))

    for step in range(half_count):
        vector = apply(vector)
        if step < half_count - 1:
            hop = [(step, step + 1), (seg_count - 1 - step, seg_count - 2 - step)]
            vector = lax.ppermute(vector, "seg", hop)

    low, high = half_count - 1, half_count
    other = lax.ppermute(vector, "seg", [(low, high), (high, low)])
    amp = jnp.sum(vector.astype(jnp.float32) * other.astype(jnp.float32), axis=1)
    at_meet = (seg_index == low) | (seg_index == high)
    amp = jnp.where(at_meet, amp, jnp.zeros_like(amp))

    tile = jnp.zeros((8, width), jnp.float32).at[0, :group].set(amp)
    tiles = lax.all_gather(tile, "sec", axis=0, tiled=False)
    full = tiles[:, 0, :group].reshape(conf_count)

    def outward(offset, holders):
        pairs = []
        for h in holders:
            target = h - offset if h <= low else h + offset
            if 0 <= target < seg_count:
                pairs.append((h, target))
        return pairs

    holders = [low, high]
    for offsets in ((1, 2, 3), (4, 8, 12)):
        full = exchange_rounds(full, "seg", [outward(o, holders) for o in offsets])
        holders = sorted(set(holders) | {t for o in offsets for _, t in outward(o, holders)})
    return full


def solution(mesh):
    in_specs = (
        P("seg", None, "sec", None, None),
        P("sec", None),
        P("sec", None),
        P(None, "seg"),
        P(),
    )
    out_specs = P()
    return jax.shard_map(
        per_device, mesh=mesh, in_specs=in_specs, out_specs=out_specs, check_vma=False
    )
```

```python
import jax
import jax.numpy as jnp
from jax import lax
from jax.sharding import PartitionSpec as P


def exchange_rounds(value, axis, partner_sets):
    total = value
    for pairs in partner_sets:
        if pairs:
            total = total + lax.ppermute(value, axis, pairs)
    return total


def per_device(blocks, left_edge, right_edge, occupation, start_sector):
    seg_count = lax.axis_size("seg")
    sec_count = lax.axis_size("sec")
    half_count = seg_count // 2
    seg_index = lax.axis_index("seg")
    sec_index = lax.axis_index("sec")
    is_left = seg_index < half_count
    depth = jnp.where(is_left, seg_index, seg_count - 1 - seg_index)

    conf_count = occupation.shape[0]
    sites = seg_count * occupation.shape[1]
    group = conf_count // sec_count
    width = blocks.shape[-1]
    local_states = blocks.shape[1]

    local = blocks[0, :, 0]
    local = jnp.where(is_left, local, jnp.swapaxes(local, 1, 2))
    edges = jnp.concatenate(
        [left_edge, right_edge, jnp.zeros((width - 2, width), blocks.dtype)], axis=0
    )
    packed = jnp.concatenate([local, edges[None]], axis=0)
    oriented = lax.all_gather(packed, "sec", axis=0, tiled=False)
    nsec = oriented.shape[0]
    lefts = oriented[:, local_states, 0]
    rights = oriented[:, local_states, 1]

    row0 = sec_index * group
    occ_mine = lax.dynamic_slice_in_dim(occupation, row0, group, axis=0)
    occ_group = lax.all_gather(occ_mine, "seg", axis=1, tiled=True)
    start_group = lax.dynamic_slice_in_dim(start_sector, row0, group, axis=0)

    charge = jnp.array([0, 1, -1, 0], dtype=jnp.int32)
    steps = charge[occ_group]
    site_ids = jnp.arange(sites, dtype=jnp.int32)
    before = jnp.sum(jnp.where(site_ids[None, :] < seg_index, steps, 0), axis=1)
    total = jnp.sum(steps, axis=1)
    sector_here = jnp.mod(start_group + before, nsec)
    sector_end = jnp.mod(start_group + total, nsec)
    occ_here = occ_mine[:, 0]

    sector_hot = (sector_here[:, None] == jnp.arange(nsec, dtype=jnp.int32)[None, :]).astype(
        jnp.bfloat16
    )
    state_hot = (occ_here[:, None] == jnp.arange(local_states + 1, dtype=jnp.int32)[None, :]).astype(
        jnp.float32
    )

    def apply(vector):
        spread = vector[:, None, :] * sector_hot[:, :, None]
        products = jnp.einsum(
            "kqa,qnab->knb", spread, oriented, preferred_element_type=jnp.float32
        )
        return jnp.sum(products * state_hot[:, :, None], axis=1).astype(jnp.bfloat16)

    first_left = jnp.take(lefts, start_group, axis=0)
    first_right = jnp.take(rights, sector_end, axis=0)
    first = jnp.where(is_left, first_left, first_right)
    vector = jnp.where(depth == 0, first, jnp.zeros_like(first))

    for step in range(half_count):
        vector = apply(vector)
        if step < half_count - 1:
            hop = [(step, step + 1), (seg_count - 1 - step, seg_count - 2 - step)]
            vector = lax.ppermute(vector, "seg", hop)

    low, high = half_count - 1, half_count
    other = lax.ppermute(vector, "seg", [(low, high), (high, low)])
    amp = jnp.sum(vector.astype(jnp.float32) * other.astype(jnp.float32), axis=1)
    at_meet = (seg_index == low) | (seg_index == high)
    amp = jnp.where(at_meet, amp, jnp.zeros_like(amp))

    pieces = amp[None, :]
    span = 1
    while span < sec_count:
        own_slot = (sec_index // span) % 4
        parts = [pieces]
        for t in (1, 2, 3):
            pairs = [
                (m * sec_count + i, m * sec_count + (i ^ (t * span)))
                for m in (low, high)
                for i in range(sec_count)
            ]
            parts.append(lax.ppermute(pieces, ("seg", "sec"), pairs))
        slots = []
        for r in range(4):
            chosen = jnp.zeros_like(pieces)
            for t in range(4):
                chosen = chosen + jnp.where(own_slot ^ t == r, parts[t], jnp.zeros_like(pieces))
            slots.append(chosen)
        pieces = jnp.concatenate(slots, axis=0)
        span *= 4
    full = pieces.reshape(conf_count)

    def outward(offset, holders):
        pairs = []
        for h in holders:
            target = h - offset if h <= low else h + offset
            if 0 <= target < seg_count:
                pairs.append((h, target))
        return pairs

    holders = [low, high]
    for offsets in ((1, 2, 3), (4, 8, 12)):
        full = exchange_rounds(full, "seg", [outward(o, holders) for o in offsets])
        holders = sorted(set(holders) | {t for o in offsets for _, t in outward(o, holders)})
    return full


def solution(mesh):
    in_specs = (
        P("seg", None, "sec", None, None),
        P("sec", None),
        P("sec", None),
        P(None, "seg"),
        P(),
    )
    out_specs = P()
    return jax.shard_map(
        per_device, mesh=mesh, in_specs=in_specs, out_specs=out_specs, check_vma=False
    )
```

```python
import jax
import jax.numpy as jnp
from jax import lax
from jax.sharding import PartitionSpec as P


def exchange_rounds(value, axis, partner_sets):
    total = value
    for pairs in partner_sets:
        if pairs:
            total = total + lax.ppermute(value, axis, pairs)
    return total


def per_device(blocks, left_edge, right_edge, occupation, start_sector):
    seg_count = lax.axis_size("seg")
    sec_count = lax.axis_size("sec")
    half_count = seg_count // 2
    seg_index = lax.axis_index("seg")
    sec_index = lax.axis_index("sec")
    is_left = seg_index < half_count
    depth = jnp.where(is_left, seg_index, seg_count - 1 - seg_index)

    conf_count = occupation.shape[0]
    sites = seg_count * occupation.shape[1]
    group = conf_count // sec_count
    width = blocks.shape[-1]
    local_states = blocks.shape[1]

    local = blocks[0, :, 0]
    local = jnp.where(is_left, local, jnp.swapaxes(local, 1, 2))
    rows = local.reshape(local_states * width, width)
    tail = jnp.zeros((14, width), blocks.dtype)
    packed = jnp.concatenate([rows, left_edge, right_edge, tail], axis=0)
    oriented = lax.all_gather(packed, "sec", axis=0, tiled=False)
    nsec = oriented.shape[0]
    body = local_states * width
    lefts = oriented[:, body]
    rights = oriented[:, body + 1]

    row0 = sec_index * group
    occ_mine = lax.dynamic_slice_in_dim(occupation, row0, group, axis=0)
    occ_group = lax.all_gather(occ_mine, "seg", axis=1, tiled=True)
    start_group = lax.dynamic_slice_in_dim(start_sector, row0, group, axis=0)

    charge = jnp.array([0, 1, -1, 0], dtype=jnp.int32)
    steps = charge[occ_group]
    site_ids = jnp.arange(sites, dtype=jnp.int32)
    before = jnp.sum(jnp.where(site_ids[None, :] < seg_index, steps, 0), axis=1)
    total = jnp.sum(steps, axis=1)
    sector_here = jnp.mod(start_group + before, nsec)
    sector_end = jnp.mod(start_group + total, nsec)
    occ_here = occ_mine[:, 0]

    sector_hot = (sector_here[:, None] == jnp.arange(nsec, dtype=jnp.int32)[None, :]).astype(
        jnp.bfloat16
    )
    state_hot = (occ_here[:, None] == jnp.arange(local_states, dtype=jnp.int32)[None, :]).astype(
        jnp.bfloat16
    )
    slot_hot = sector_hot[:, :, None] * state_hot[:, None, :]

    def apply(vector):
        spread = slot_hot[:, :, :, None] * vector[:, None, None, :]
        spread = spread.reshape(group, nsec, body)
        spread = jnp.pad(spread, ((0, 0), (0, 0), (0, oriented.shape[1] - body)))
        products = jnp.einsum(
            "kqr,qrb->kb", spread, oriented, preferred_element_type=jnp.float32
        )
        return products.astype(jnp.bfloat16)

    first_left = jnp.take(lefts, start_group, axis=0)
    first_right = jnp.take(rights, sector_end, axis=0)
    first = jnp.where(is_left, first_left, first_right)
    vector = jnp.where(depth == 0, first, jnp.zeros_like(first))

    for step in range(half_count):
        vector = apply(vector)
        if step < half_count - 1:
            hop = [(step, step + 1), (seg_count - 1 - step, seg_count - 2 - step)]
            vector = lax.ppermute(vector, "seg", hop)

    low, high = half_count - 1, half_count
    other = lax.ppermute(vector, "seg", [(low, high), (high, low)])
    amp = jnp.sum(vector.astype(jnp.float32) * other.astype(jnp.float32), axis=1)
    at_meet = (seg_index == low) | (seg_index == high)
    amp = jnp.where(at_meet, amp, jnp.zeros_like(amp))

    tile = jnp.zeros((8, width), jnp.float32).at[0, :group].set(amp)
    tiles = lax.all_gather(tile, "sec", axis=0, tiled=False)
    full = tiles[:, 0, :group].reshape(conf_count)

    def outward(offset, holders):
        pairs = []
        for h in holders:
            target = h - offset if h <= low else h + offset
            if 0 <= target < seg_count:
                pairs.append((h, target))
        return pairs

    holders = [low, high]
    for offsets in ((1, 2, 3), (4, 8, 12)):
        full = exchange_rounds(full, "seg", [outward(o, holders) for o in offsets])
        holders = sorted(set(holders) | {t for o in offsets for _, t in outward(o, holders)})
    return full


def solution(mesh):
    in_specs = (
        P("seg", None, "sec", None, None),
        P("sec", None),
        P("sec", None),
        P(None, "seg"),
        P(),
    )
    out_specs = P()
    return jax.shard_map(
        per_device, mesh=mesh, in_specs=in_specs, out_specs=out_specs, check_vma=False
    )
```

```python
import jax
import jax.numpy as jnp
from jax import lax
from jax.sharding import PartitionSpec as P


def spread_pairs(holders, count, fan):
    have = sorted(holders)
    rounds = []
    while len(have) < count:
        missing = [i for i in range(count) if i not in have]
        perms = []
        for _ in range(fan):
            pairs = []
            for h in have:
                if not missing:
                    break
                target = min(missing, key=lambda m: (abs(m - h), m))
                missing.remove(target)
                pairs.append((h, target))
            if pairs:
                perms.append(pairs)
        rounds.append(perms)
        have = sorted(set(have) | {t for perm in perms for _, t in perm})
    return rounds


def per_device(blocks, left_edge, right_edge, occupation, start_sector):
    seg_count = lax.axis_size("seg")
    sec_count = lax.axis_size("sec")
    half_count = seg_count // 2
    seg_index = lax.axis_index("seg")
    sec_index = lax.axis_index("sec")
    is_left = seg_index < half_count

    conf_count = occupation.shape[0]
    sites = seg_count * occupation.shape[1]
    group = conf_count // sec_count
    width = blocks.shape[-1]
    local_states = blocks.shape[1]

    partner = seg_index ^ 1
    depth = jnp.where(is_left, seg_index // 2, (seg_count - 1 - seg_index) // 2)

    local = blocks[0, :, 0]
    local = jnp.where(is_left, local, jnp.swapaxes(local, 1, 2))
    feed = [(2 * m + 1, 2 * m) for m in range(half_count // 2)] + [
        (2 * m, 2 * m + 1) for m in range(half_count // 2, seg_count // 2)
    ]
    partner_local = lax.ppermute(local, "seg", feed)
    tail = jnp.zeros((14, width), blocks.dtype)
    body = local_states * width

    def site_rows(part):
        rows = part.reshape(body, width)
        return jnp.concatenate([rows, left_edge, right_edge, tail], axis=0)

    packed = jnp.stack([site_rows(local), site_rows(partner_local)], axis=0)
    both = lax.all_gather(packed, "sec", axis=1, tiled=False)
    nsec = both.shape[1]
    lefts = both[0, :, body]
    rights = both[0, :, body + 1]

    row0 = sec_index * group
    occ_mine = lax.dynamic_slice_in_dim(occupation, row0, group, axis=0)
    occ_group = lax.all_gather(occ_mine, "seg", axis=1, tiled=True)
    start_group = lax.dynamic_slice_in_dim(start_sector, row0, group, axis=0)

    charge = jnp.array([0, 1, -1, 0], dtype=jnp.int32)
    steps = charge[occ_group]
    site_ids = jnp.arange(sites, dtype=jnp.int32)
    total = jnp.sum(steps, axis=1)
    sector_end = jnp.mod(start_group + total, nsec)
    sector_ids = jnp.arange(nsec, dtype=jnp.int32)
    state_ids = jnp.arange(local_states, dtype=jnp.int32)

    def site_slots(site):
        before = jnp.sum(jnp.where(site_ids[None, :] < site, steps, 0), axis=1)
        sector = jnp.mod(start_group + before, nsec)
        occ = jnp.sum(jnp.where(site_ids[None, :] == site, occ_group, 0), axis=1)
        sector_hot = (sector[:, None] == sector_ids[None, :]).astype(jnp.bfloat16)
        state_hot = (occ[:, None] == state_ids[None, :]).astype(jnp.bfloat16)
        return sector_hot[:, :, None] * state_hot[:, None, :]

    slots = [site_slots(seg_index), site_slots(partner)]

    def apply(vector, which):
        spread = slots[which][:, :, :, None] * vector[:, None, None, :]
        spread = spread.reshape(group, nsec, body)
        spread = jnp.pad(spread, ((0, 0), (0, 0), (0, both.shape[2] - body)))
        products = jnp.einsum(
            "kqr,qrb->kb", spread, both[which], preferred_element_type=jnp.float32
        )
        return products.astype(jnp.bfloat16)

    first_left = jnp.take(lefts, start_group, axis=0)
    first_right = jnp.take(rights, sector_end, axis=0)
    first = jnp.where(is_left, first_left, first_right)
    vector = jnp.where(depth == 0, first, jnp.zeros_like(first))

    chain_steps = half_count // 2
    for step in range(chain_steps):
        vector = apply(vector, 0)
        vector = apply(vector, 1)
        if step < chain_steps - 1:
            hop = [(2 * step, 2 * step + 2), (seg_count - 1 - 2 * step, seg_count - 3 - 2 * step)]
            vector = lax.ppermute(vector, "seg", hop)

    low, high = half_count - 2, half_count + 1
    other = lax.ppermute(vector, "seg", [(low, high), (high, low)])
    amp = jnp.sum(vector.astype(jnp.float32) * other.astype(jnp.float32), axis=1)
    at_meet = (seg_index == low) | (seg_index == high)
    amp = jnp.where(at_meet, amp, jnp.zeros_like(amp))

    tile = jnp.zeros((8, width), jnp.float32).at[0, :group].set(amp)
    tiles = lax.all_gather(tile, "sec", axis=0, tiled=False)
    full = tiles[:, 0, :group].reshape(conf_count)

    for perms in spread_pairs([low, high], seg_count, 3):
        received = [lax.ppermute(full, "seg", pairs) for pairs in perms]
        for value in received:
            full = full + value
    return full


def solution(mesh):
    in_specs = (
        P("seg", None, "sec", None, None),
        P("sec", None),
        P("sec", None),
        P(None, "seg"),
        P(),
    )
    out_specs = P()
    return jax.shard_map(
        per_device, mesh=mesh, in_specs=in_specs, out_specs=out_specs, check_vma=False
    )
```

```python
import jax
import jax.numpy as jnp
from jax import lax
from jax.sharding import PartitionSpec as P

SITES_PER_DEVICE = 4


def spread_pairs(holders, count, fan):
    have = sorted(holders)
    rounds = []
    while len(have) < count:
        missing = [i for i in range(count) if i not in have]
        perms = []
        for _ in range(fan):
            pairs = []
            for h in have:
                if not missing:
                    break
                target = min(missing, key=lambda m: (abs(m - h), m))
                missing.remove(target)
                pairs.append((h, target))
            if pairs:
                perms.append(pairs)
        rounds.append(perms)
        have = sorted(set(have) | {t for perm in perms for _, t in perm})
    return rounds


def per_device(blocks, left_edge, right_edge, occupation, start_sector):
    seg_count = lax.axis_size("seg")
    sec_count = lax.axis_size("sec")
    half_count = seg_count // 2
    seg_index = lax.axis_index("seg")
    sec_index = lax.axis_index("sec")
    is_left = seg_index < half_count

    conf_count = occupation.shape[0]
    sites = seg_count * occupation.shape[1]
    group = conf_count // sec_count
    width = blocks.shape[-1]
    local_states = blocks.shape[1]

    span = SITES_PER_DEVICE
    direction = jnp.where(is_left, 1, -1)
    depth = jnp.where(is_left, seg_index // span, (seg_count - 1 - seg_index) // span)

    local = blocks[0, :, 0]
    local = jnp.where(is_left, local, jnp.swapaxes(local, 1, 2))
    runs = seg_count // span
    parts = [local]
    for t in range(1, span):
        feed = [(r * span + t, r * span) for r in range(runs // 2)] + [
            (r * span + span - 1 - t, r * span + span - 1) for r in range(runs // 2, runs)
        ]
        parts.append(lax.ppermute(local, "seg", feed))
    tail = jnp.zeros((14, width), blocks.dtype)
    body = local_states * width

    def site_rows(part):
        rows = part.reshape(body, width)
        return jnp.concatenate([rows, left_edge, right_edge, tail], axis=0)

    packed = jnp.stack([site_rows(part) for part in parts], axis=0)
    both = lax.all_gather(packed, "sec", axis=1, tiled=False)
    nsec = both.shape[1]
    lefts = both[0, :, body]
    rights = both[0, :, body + 1]

    row0 = sec_index * group
    occ_mine = lax.dynamic_slice_in_dim(occupation, row0, group, axis=0)
    occ_group = lax.all_gather(occ_mine, "seg", axis=1, tiled=True)
    start_group = lax.dynamic_slice_in_dim(start_sector, row0, group, axis=0)

    charge = jnp.array([0, 1, -1, 0], dtype=jnp.int32)
    steps = charge[occ_group]
    site_ids = jnp.arange(sites, dtype=jnp.int32)
    total = jnp.sum(steps, axis=1)
    sector_end = jnp.mod(start_group + total, nsec)
    sector_ids = jnp.arange(nsec, dtype=jnp.int32)
    state_ids = jnp.arange(local_states, dtype=jnp.int32)

    def site_slots(site):
        before = jnp.sum(jnp.where(site_ids[None, :] < site, steps, 0), axis=1)
        sector = jnp.mod(start_group + before, nsec)
        occ = jnp.sum(jnp.where(site_ids[None, :] == site, occ_group, 0), axis=1)
        sector_hot = (sector[:, None] == sector_ids[None, :]).astype(jnp.bfloat16)
        state_hot = (occ[:, None] == state_ids[None, :]).astype(jnp.bfloat16)
        return sector_hot[:, :, None] * state_hot[:, None, :]

    slots = [site_slots(seg_index + t * direction) for t in range(span)]

    def apply(vector, which):
        spread = slots[which][:, :, :, None] * vector[:, None, None, :]
        spread = spread.reshape(group, nsec, body)
        spread = jnp.pad(spread, ((0, 0), (0, 0), (0, both.shape[2] - body)))
        products = jnp.einsum(
            "kqr,qrb->kb", spread, both[which], preferred_element_type=jnp.float32
        )
        return products.astype(jnp.bfloat16)

    first_left = jnp.take(lefts, start_group, axis=0)
    first_right = jnp.take(rights, sector_end, axis=0)
    first = jnp.where(is_left, first_left, first_right)
    vector = jnp.where(depth == 0, first, jnp.zeros_like(first))

    chain_steps = half_count // span
    for step in range(chain_steps):
        for t in range(span):
            vector = apply(vector, t)
        if step < chain_steps - 1:
            hop = [
                (span * step, span * (step + 1)),
                (seg_count - 1 - span * step, seg_count - 1 - span * (step + 1)),
            ]
            vector = lax.ppermute(vector, "seg", hop)

    low, high = half_count - span, half_count + span - 1
    other = lax.ppermute(vector, "seg", [(low, high), (high, low)])
    amp = jnp.sum(vector.astype(jnp.float32) * other.astype(jnp.float32), axis=1)
    at_meet = (seg_index == low) | (seg_index == high)
    amp = jnp.where(at_meet, amp, jnp.zeros_like(amp))

    tile = jnp.zeros((8, width), jnp.float32).at[0, :group].set(amp)
    tiles = lax.all_gather(tile, "sec", axis=0, tiled=False)
    full = tiles[:, 0, :group].reshape(conf_count)

    for perms in spread_pairs([low, high], seg_count, 3):
        received = [lax.ppermute(full, "seg", pairs) for pairs in perms]
        for value in received:
            full = full + value
    return full


def solution(mesh):
    in_specs = (
        P("seg", None, "sec", None, None),
        P("sec", None),
        P("sec", None),
        P(None, "seg"),
        P(),
    )
    out_specs = P()
    return jax.shard_map(
        per_device, mesh=mesh, in_specs=in_specs, out_specs=out_specs, check_vma=False
    )
```

```python
import jax
import jax.numpy as jnp
from jax import lax
from jax.sharding import PartitionSpec as P

SITES_PER_DEVICE = 4


def spread_pairs(holders, count, fan):
    have = sorted(holders)
    rounds = []
    while len(have) < count:
        missing = [i for i in range(count) if i not in have]
        perms = []
        for _ in range(fan):
            pairs = []
            for h in have:
                if not missing:
                    break
                target = min(missing, key=lambda m: (abs(m - h), m))
                missing.remove(target)
                pairs.append((h, target))
            if pairs:
                perms.append(pairs)
        rounds.append(perms)
        have = sorted(set(have) | {t for perm in perms for _, t in perm})
    return rounds


def per_device(blocks, left_edge, right_edge, occupation, start_sector):
    seg_count = lax.axis_size("seg")
    sec_count = lax.axis_size("sec")
    half_count = seg_count // 2
    seg_index = lax.axis_index("seg")
    sec_index = lax.axis_index("sec")
    is_left = seg_index < half_count

    conf_count = occupation.shape[0]
    sites = seg_count * occupation.shape[1]
    group = conf_count // sec_count
    width = blocks.shape[-1]
    local_states = blocks.shape[1]

    span = SITES_PER_DEVICE
    direction = jnp.where(is_left, 1, -1)
    depth = jnp.where(is_left, seg_index // span, (seg_count - 1 - seg_index) // span)

    local = blocks[0, :, 0]
    local = jnp.where(is_left, local, jnp.swapaxes(local, 1, 2))
    runs = seg_count // span
    parts = [local]
    for t in range(1, span):
        feed = [(r * span + t, r * span) for r in range(runs // 2)] + [
            (r * span + span - 1 - t, r * span + span - 1) for r in range(runs // 2, runs)
        ]
        parts.append(lax.ppermute(local, "seg", feed))
    tail = jnp.zeros((14, width), blocks.dtype)
    body = local_states * width

    def site_rows(part):
        rows = part.reshape(body, width)
        return jnp.concatenate([rows, left_edge, right_edge, tail], axis=0)

    packed = jnp.stack([site_rows(part) for part in parts], axis=0)
    gathered = lax.all_gather(packed, "sec", axis=0, tiled=False)
    nsec = gathered.shape[0]
    both = [gathered[:, t] for t in range(span)]
    lefts = gathered[:, 0, body]
    rights = gathered[:, 0, body + 1]

    row0 = sec_index * group
    occ_mine = lax.dynamic_slice_in_dim(occupation, row0, group, axis=0)
    occ_group = lax.all_gather(occ_mine, "seg", axis=1, tiled=True)
    start_group = lax.dynamic_slice_in_dim(start_sector, row0, group, axis=0)

    charge = jnp.array([0, 1, -1, 0], dtype=jnp.int32)
    steps = charge[occ_group]
    site_ids = jnp.arange(sites, dtype=jnp.int32)
    total = jnp.sum(steps, axis=1)
    sector_end = jnp.mod(start_group + total, nsec)
    sector_ids = jnp.arange(nsec, dtype=jnp.int32)
    state_ids = jnp.arange(local_states, dtype=jnp.int32)

    def site_slots(site):
        before = jnp.sum(jnp.where(site_ids[None, :] < site, steps, 0), axis=1)
        sector = jnp.mod(start_group + before, nsec)
        occ = jnp.sum(jnp.where(site_ids[None, :] == site, occ_group, 0), axis=1)
        sector_hot = (sector[:, None] == sector_ids[None, :]).astype(jnp.bfloat16)
        state_hot = (occ[:, None] == state_ids[None, :]).astype(jnp.bfloat16)
        return sector_hot[:, :, None] * state_hot[:, None, :]

    slots = [site_slots(seg_index + t * direction) for t in range(span)]

    def apply(vector, which):
        spread = slots[which][:, :, :, None] * vector[:, None, None, :]
        spread = spread.reshape(group, nsec, body)
        spread = jnp.pad(spread, ((0, 0), (0, 0), (0, both[which].shape[1] - body)))
        products = jnp.einsum(
            "kqr,qrb->kb", spread, both[which], preferred_element_type=jnp.float32
        )
        return products.astype(jnp.bfloat16)

    first_left = jnp.take(lefts, start_group, axis=0)
    first_right = jnp.take(rights, sector_end, axis=0)
    first = jnp.where(is_left, first_left, first_right)
    vector = jnp.where(depth == 0, first, jnp.zeros_like(first))

    chain_steps = half_count // span
    for step in range(chain_steps):
        for t in range(span):
            vector = apply(vector, t)
        if step < chain_steps - 1:
            hop = [
                (span * step, span * (step + 1)),
                (seg_count - 1 - span * step, seg_count - 1 - span * (step + 1)),
            ]
            vector = lax.ppermute(vector, "seg", hop)

    low, high = half_count - span, half_count + span - 1
    other = lax.ppermute(vector, "seg", [(low, high), (high, low)])
    amp = jnp.sum(vector.astype(jnp.float32) * other.astype(jnp.float32), axis=1)
    at_meet = (seg_index == low) | (seg_index == high)
    amp = jnp.where(at_meet, amp, jnp.zeros_like(amp))

    tile = jnp.zeros((8, width), jnp.float32).at[0, :group].set(amp)
    tiles = lax.all_gather(tile, "sec", axis=0, tiled=False)
    full = tiles[:, 0, :group].reshape(conf_count)

    for perms in spread_pairs([low, high], seg_count, 3):
        received = [lax.ppermute(full, "seg", pairs) for pairs in perms]
        for value in received:
            full = full + value
    return full


def solution(mesh):
    in_specs = (
        P("seg", None, "sec", None, None),
        P("sec", None),
        P("sec", None),
        P(None, "seg"),
        P(),
    )
    out_specs = P()
    return jax.shard_map(
        per_device, mesh=mesh, in_specs=in_specs, out_specs=out_specs, check_vma=False
    )
```

```python
import jax
import jax.numpy as jnp
from jax import lax
from jax.sharding import PartitionSpec as P

SITES_PER_DEVICE = 4


def spread_pairs(holders, count, fan):
    have = sorted(holders)
    rounds = []
    while len(have) < count:
        missing = [i for i in range(count) if i not in have]
        perms = []
        for _ in range(fan):
            pairs = []
            for h in have:
                if not missing:
                    break
                target = min(missing, key=lambda m: (abs(m - h), m))
                missing.remove(target)
                pairs.append((h, target))
            if pairs:
                perms.append(pairs)
        rounds.append(perms)
        have = sorted(set(have) | {t for perm in perms for _, t in perm})
    return rounds


def per_device(blocks, left_edge, right_edge, occupation, start_sector):
    seg_count = lax.axis_size("seg")
    sec_count = lax.axis_size("sec")
    half_count = seg_count // 2
    seg_index = lax.axis_index("seg")
    sec_index = lax.axis_index("sec")
    is_left = seg_index < half_count

    conf_count = occupation.shape[0]
    sites = seg_count * occupation.shape[1]
    group = conf_count // sec_count
    width = blocks.shape[-1]
    local_states = blocks.shape[1]

    span = SITES_PER_DEVICE
    direction = jnp.where(is_left, 1, -1)
    depth = jnp.where(is_left, seg_index // span, (seg_count - 1 - seg_index) // span)

    local = blocks[0, :, 0]
    local = jnp.where(is_left, local, jnp.swapaxes(local, 1, 2))
    runs = seg_count // span
    parts = [local]
    for t in range(1, span):
        feed = [(r * span + t, r * span) for r in range(runs // 2)] + [
            (r * span + span - 1 - t, r * span + span - 1) for r in range(runs // 2, runs)
        ]
        parts.append(lax.ppermute(local, "seg", feed))
    tail = jnp.zeros((14, width), blocks.dtype)
    body = local_states * width

    def site_rows(part):
        rows = part.reshape(body, width)
        return jnp.concatenate([rows, left_edge, right_edge, tail], axis=0)

    packed = jnp.stack([site_rows(part) for part in parts], axis=0)
    gathered = lax.all_gather(packed, "sec", axis=0, tiled=False)
    nsec = gathered.shape[0]
    both = [gathered[:, t] for t in range(span)]
    lefts = gathered[:, 0, body]
    rights = gathered[:, 0, body + 1]

    row0 = sec_index * group
    occ_mine = lax.dynamic_slice_in_dim(occupation, row0, group, axis=0)
    occ_group = lax.all_gather(occ_mine, "seg", axis=1, tiled=True)
    start_group = lax.dynamic_slice_in_dim(start_sector, row0, group, axis=0)

    charge = jnp.array([0, 1, -1, 0], dtype=jnp.int32)
    steps = charge[occ_group]
    site_ids = jnp.arange(sites, dtype=jnp.int32)
    total = jnp.sum(steps, axis=1)
    sector_end = jnp.mod(start_group + total, nsec)
    sector_ids = jnp.arange(nsec, dtype=jnp.int32)
    state_ids = jnp.arange(local_states, dtype=jnp.int32)

    def site_slots(site):
        before = jnp.sum(jnp.where(site_ids[None, :] < site, steps, 0), axis=1)
        sector = jnp.mod(start_group + before, nsec)
        occ = jnp.sum(jnp.where(site_ids[None, :] == site, occ_group, 0), axis=1)
        sector_hot = (sector[:, None] == sector_ids[None, :]).astype(jnp.bfloat16)
        state_hot = (occ[:, None] == state_ids[None, :]).astype(jnp.bfloat16)
        return sector_hot[:, :, None] * state_hot[:, None, :]

    slots = [site_slots(seg_index + t * direction) for t in range(span)]

    def apply(vector, which):
        spread = slots[which][:, :, :, None] * vector[:, None, None, :]
        spread = spread.reshape(group, nsec, body)
        spread = jnp.pad(spread, ((0, 0), (0, 0), (0, both[which].shape[1] - body)))
        products = jnp.einsum(
            "kqr,qrb->kb", spread, both[which], preferred_element_type=jnp.float32
        )
        return products.astype(jnp.bfloat16)

    first_sector = jnp.where(is_left, start_group, sector_end)
    first_hot = (first_sector[:, None] == sector_ids[None, :]).astype(jnp.bfloat16)
    edge_rows = jnp.where(is_left, lefts, rights)
    first = jnp.einsum(
        "kq,qa->ka", first_hot, edge_rows, preferred_element_type=jnp.float32
    ).astype(jnp.bfloat16)
    vector = jnp.where(depth == 0, first, jnp.zeros_like(first))

    chain_steps = half_count // span
    for step in range(chain_steps):
        for t in range(span):
            vector = apply(vector, t)
        if step < chain_steps - 1:
            hop = [
                (span * step, span * (step + 1)),
                (seg_count - 1 - span * step, seg_count - 1 - span * (step + 1)),
            ]
            vector = lax.ppermute(vector, "seg", hop)

    low, high = half_count - span, half_count + span - 1
    other = lax.ppermute(vector, "seg", [(low, high), (high, low)])
    amp = jnp.sum(vector.astype(jnp.float32) * other.astype(jnp.float32), axis=1)
    at_meet = (seg_index == low) | (seg_index == high)
    amp = jnp.where(at_meet, amp, jnp.zeros_like(amp))

    tile = jnp.zeros((8, width), jnp.float32).at[0, :group].set(amp)
    tiles = lax.all_gather(tile, "sec", axis=0, tiled=False)
    full = tiles[:, 0, :group].reshape(conf_count)

    for perms in spread_pairs([low, high], seg_count, 3):
        received = [lax.ppermute(full, "seg", pairs) for pairs in perms]
        for value in received:
            full = full + value
    return full


def solution(mesh):
    in_specs = (
        P("seg", None, "sec", None, None),
        P("sec", None),
        P("sec", None),
        P(None, "seg"),
        P(),
    )
    out_specs = P()
    return jax.shard_map(
        per_device, mesh=mesh, in_specs=in_specs, out_specs=out_specs, check_vma=False
    )
```

```python
import jax
import jax.numpy as jnp
from jax import lax
from jax.sharding import PartitionSpec as P

SITES_PER_DEVICE = 4


def spread_pairs(holders, count, fan):
    have = sorted(holders)
    rounds = []
    while len(have) < count:
        missing = [i for i in range(count) if i not in have]
        perms = []
        for _ in range(fan):
            pairs = []
            for h in have:
                if not missing:
                    break
                target = min(missing, key=lambda m: (abs(m - h), m))
                missing.remove(target)
                pairs.append((h, target))
            if pairs:
                perms.append(pairs)
        rounds.append(perms)
        have = sorted(set(have) | {t for perm in perms for _, t in perm})
    return rounds


def per_device(blocks, left_edge, right_edge, occupation, start_sector):
    seg_count = lax.axis_size("seg")
    sec_count = lax.axis_size("sec")
    half_count = seg_count // 2
    seg_index = lax.axis_index("seg")
    sec_index = lax.axis_index("sec")
    is_left = seg_index < half_count

    conf_count = occupation.shape[0]
    sites = seg_count * occupation.shape[1]
    group = conf_count // sec_count
    width = blocks.shape[-1]
    local_states = blocks.shape[1]

    span = SITES_PER_DEVICE
    direction = jnp.where(is_left, 1, -1)
    depth = jnp.where(is_left, seg_index // span, (seg_count - 1 - seg_index) // span)

    local = blocks[0, :, 0]
    local = jnp.where(is_left, local, jnp.swapaxes(local, 1, 2))
    runs = seg_count // span
    parts = [local]
    for t in range(1, span):
        feed = [(r * span + t, r * span) for r in range(runs // 2)] + [
            (r * span + span - 1 - t, r * span + span - 1) for r in range(runs // 2, runs)
        ]
        parts.append(lax.ppermute(local, "seg", feed))
    tail = jnp.zeros((14, width), blocks.dtype)
    body = local_states * width

    def site_rows(part):
        rows = part.reshape(body, width)
        return jnp.concatenate([rows, left_edge, right_edge, tail], axis=0)

    packed = jnp.stack([site_rows(part) for part in parts], axis=0)
    gathered = lax.all_gather(packed, "sec", axis=1, tiled=False)
    nsec = gathered.shape[1]
    both = [gathered[t] for t in range(span)]
    lefts = gathered[0, :, body]
    rights = gathered[0, :, body + 1]

    row0 = sec_index * group
    occ_mine = lax.dynamic_slice_in_dim(occupation, row0, group, axis=0)
    occ_group = lax.all_gather(occ_mine, "seg", axis=1, tiled=True)
    start_group = lax.dynamic_slice_in_dim(start_sector, row0, group, axis=0)

    charge = jnp.array([0, 1, -1, 0], dtype=jnp.int32)
    steps = charge[occ_group]
    site_ids = jnp.arange(sites, dtype=jnp.int32)
    total = jnp.sum(steps, axis=1)
    sector_end = jnp.mod(start_group + total, nsec)
    sector_ids = jnp.arange(nsec, dtype=jnp.int32)
    state_ids = jnp.arange(local_states, dtype=jnp.int32)

    def site_slots(site):
        before = jnp.sum(jnp.where(site_ids[None, :] < site, steps, 0), axis=1)
        sector = jnp.mod(start_group + before, nsec)
        occ = jnp.sum(jnp.where(site_ids[None, :] == site, occ_group, 0), axis=1)
        sector_hot = (sector[:, None] == sector_ids[None, :]).astype(jnp.bfloat16)
        state_hot = (occ[:, None] == state_ids[None, :]).astype(jnp.bfloat16)
        return sector_hot[:, :, None] * state_hot[:, None, :]

    slots = [site_slots(seg_index + t * direction) for t in range(span)]

    def apply(vector, which):
        spread = slots[which][:, :, :, None] * vector[:, None, None, :]
        spread = spread.reshape(group, nsec, body)
        spread = jnp.pad(spread, ((0, 0), (0, 0), (0, both[which].shape[1] - body)))
        products = jnp.einsum(
            "kqr,qrb->kb", spread, both[which], preferred_element_type=jnp.float32
        )
        return products.astype(jnp.bfloat16)

    first_sector = jnp.where(is_left, start_group, sector_end)
    first_hot = (first_sector[:, None] == sector_ids[None, :]).astype(jnp.bfloat16)
    edge_rows = jnp.where(is_left, lefts, rights)
    first = jnp.einsum(
        "kq,qa->ka", first_hot, edge_rows, preferred_element_type=jnp.float32
    ).astype(jnp.bfloat16)
    vector = jnp.where(depth == 0, first, jnp.zeros_like(first))

    chain_steps = half_count // span
    for step in range(chain_steps):
        for t in range(span):
            vector = apply(vector, t)
        if step < chain_steps - 1:
            hop = [
                (span * step, span * (step + 1)),
                (seg_count - 1 - span * step, seg_count - 1 - span * (step + 1)),
            ]
            vector = lax.ppermute(vector, "seg", hop)

    low, high = half_count - span, half_count + span - 1
    other = lax.ppermute(vector, "seg", [(low, high), (high, low)])
    amp = jnp.sum(vector.astype(jnp.float32) * other.astype(jnp.float32), axis=1)
    at_meet = (seg_index == low) | (seg_index == high)
    amp = jnp.where(at_meet, amp, jnp.zeros_like(amp))

    tile = jnp.zeros((8, width), jnp.float32).at[0, :group].set(amp)
    tiles = lax.all_gather(tile, "sec", axis=0, tiled=False)
    full = tiles[:, 0, :group].reshape(conf_count)

    for perms in spread_pairs([low, high], seg_count, 3):
        received = [lax.ppermute(full, "seg", pairs) for pairs in perms]
        for value in received:
            full = full + value
    return full


def solution(mesh):
    in_specs = (
        P("seg", None, "sec", None, None),
        P("sec", None),
        P("sec", None),
        P(None, "seg"),
        P(),
    )
    out_specs = P()
    return jax.shard_map(
        per_device, mesh=mesh, in_specs=in_specs, out_specs=out_specs, check_vma=False
    )
```

```python
import jax
import jax.numpy as jnp
from jax import lax
from jax.sharding import PartitionSpec as P

SITES_PER_DEVICE = 4


def spread_pairs(holders, count, fan):
    have = sorted(holders)
    rounds = []
    while len(have) < count:
        missing = [i for i in range(count) if i not in have]
        perms = []
        for _ in range(fan):
            pairs = []
            for h in have:
                if not missing:
                    break
                target = min(missing, key=lambda m: (abs(m - h), m))
                missing.remove(target)
                pairs.append((h, target))
            if pairs:
                perms.append(pairs)
        rounds.append(perms)
        have = sorted(set(have) | {t for perm in perms for _, t in perm})
    return rounds


def per_device(blocks, left_edge, right_edge, occupation, start_sector):
    seg_count = lax.axis_size("seg")
    sec_count = lax.axis_size("sec")
    half_count = seg_count // 2
    seg_index = lax.axis_index("seg")
    sec_index = lax.axis_index("sec")
    is_left = seg_index < half_count

    conf_count = occupation.shape[0]
    sites = seg_count * occupation.shape[1]
    group = conf_count // sec_count
    width = blocks.shape[-1]
    local_states = blocks.shape[1]

    span = SITES_PER_DEVICE
    direction = jnp.where(is_left, 1, -1)
    depth = jnp.where(is_left, seg_index // span, (seg_count - 1 - seg_index) // span)

    local = blocks[0, :, 0]
    local = lax.cond(is_left, lambda x: x, lambda x: jnp.swapaxes(x, 1, 2), local)
    runs = seg_count // span
    parts = [local]
    for t in range(1, span):
        feed = [(r * span + t, r * span) for r in range(runs // 2)] + [
            (r * span + span - 1 - t, r * span + span - 1) for r in range(runs // 2, runs)
        ]
        parts.append(lax.ppermute(local, "seg", feed))
    tail = jnp.zeros((14, width), blocks.dtype)
    body = local_states * width

    def site_rows(part):
        rows = part.reshape(body, width)
        return jnp.concatenate([rows, left_edge, right_edge, tail], axis=0)

    packed = jnp.stack([site_rows(part) for part in parts], axis=0)
    gathered = lax.all_gather(packed, "sec", axis=0, tiled=False)
    nsec = gathered.shape[0]
    both = [gathered[:, t] for t in range(span)]
    lefts = gathered[:, 0, body]
    rights = gathered[:, 0, body + 1]

    row0 = sec_index * group
    occ_mine = lax.dynamic_slice_in_dim(occupation, row0, group, axis=0)
    occ_group = lax.all_gather(occ_mine, "seg", axis=1, tiled=True)
    start_group = lax.dynamic_slice_in_dim(start_sector, row0, group, axis=0)

    charge = jnp.array([0, 1, -1, 0], dtype=jnp.int32)
    steps = charge[occ_group]
    site_ids = jnp.arange(sites, dtype=jnp.int32)
    total = jnp.sum(steps, axis=1)
    sector_end = jnp.mod(start_group + total, nsec)
    sector_ids = jnp.arange(nsec, dtype=jnp.int32)
    state_ids = jnp.arange(local_states, dtype=jnp.int32)

    def site_slots(site):
        before = jnp.sum(jnp.where(site_ids[None, :] < site, steps, 0), axis=1)
        sector = jnp.mod(start_group + before, nsec)
        occ = jnp.sum(jnp.where(site_ids[None, :] == site, occ_group, 0), axis=1)
        sector_hot = (sector[:, None] == sector_ids[None, :]).astype(jnp.bfloat16)
        state_hot = (occ[:, None] == state_ids[None, :]).astype(jnp.bfloat16)
        return sector_hot[:, :, None] * state_hot[:, None, :]

    slots = [site_slots(seg_index + t * direction) for t in range(span)]

    def apply(vector, which):
        spread = slots[which][:, :, :, None] * vector[:, None, None, :]
        spread = spread.reshape(group, nsec, body)
        spread = jnp.pad(spread, ((0, 0), (0, 0), (0, both[which].shape[1] - body)))
        products = jnp.einsum(
            "kqr,qrb->kb", spread, both[which], preferred_element_type=jnp.float32
        )
        return products.astype(jnp.bfloat16)

    first_sector = jnp.where(is_left, start_group, sector_end)
    first_hot = (first_sector[:, None] == sector_ids[None, :]).astype(jnp.bfloat16)
    edge_rows = jnp.where(is_left, lefts, rights)
    first = jnp.einsum(
        "kq,qa->ka", first_hot, edge_rows, preferred_element_type=jnp.float32
    ).astype(jnp.bfloat16)
    vector = jnp.where(depth == 0, first, jnp.zeros_like(first))

    chain_steps = half_count // span
    for step in range(chain_steps):
        for t in range(span):
            vector = apply(vector, t)
        if step < chain_steps - 1:
            hop = [
                (span * step, span * (step + 1)),
                (seg_count - 1 - span * step, seg_count - 1 - span * (step + 1)),
            ]
            vector = lax.ppermute(vector, "seg", hop)

    low, high = half_count - span, half_count + span - 1
    other = lax.ppermute(vector, "seg", [(low, high), (high, low)])
    amp = jnp.sum(vector.astype(jnp.float32) * other.astype(jnp.float32), axis=1)
    at_meet = (seg_index == low) | (seg_index == high)
    amp = jnp.where(at_meet, amp, jnp.zeros_like(amp))

    tile = jnp.zeros((8, width), jnp.float32).at[0, :group].set(amp)
    tiles = lax.all_gather(tile, "sec", axis=0, tiled=False)
    full = tiles[:, 0, :group].reshape(conf_count)

    for perms in spread_pairs([low, high], seg_count, 3):
        received = [lax.ppermute(full, "seg", pairs) for pairs in perms]
        for value in received:
            full = full + value
    return full


def solution(mesh):
    in_specs = (
        P("seg", None, "sec", None, None),
        P("sec", None),
        P("sec", None),
        P(None, "seg"),
        P(),
    )
    out_specs = P()
    return jax.shard_map(
        per_device, mesh=mesh, in_specs=in_specs, out_specs=out_specs, check_vma=False
    )
```
